256 devices in a mesh: dp: 4 (over x_lo, core), expert: 64 (over z, y, x_hi).
Axes of the slice: x: 4 (x_hi: 2, x_lo: 2; x = x_hi * 2 + x_lo), y: 4, z: 8, core: 2. Of those that a mesh axis runs over, the one named last changes fastest.
Arguments:
- tokens: bfloat16 [65536, 3584], P(('dp', 'expert')), may hold values from -6 to 6
- cotangent: bfloat16 [65536, 3584], P(('dp', 'expert')), may hold values from -0.59765625 to 0.59765625
- expert_ids: int32 [65536, 1], P(('dp', 'expert')), may hold values from 0 to 63; in each aligned block of 256 rows (0 to 255, 256 to 511, ...) at most 6 rows name the same one
- gates: float32 [65536, 1], P(('dp', 'expert')), may hold values from 0.2 to 1
- pair_flags: int32 [64], replicated, may hold values from 0 to 1, as said below
- w_in: bfloat16 [64, 3584, 1024], P('expert', None, 'dp'), may hold values from -0.09375 to 0.09375
- w_out: bfloat16 [64, 1024, 3584], P('expert', 'dp'), may hold values from -0.1875 to 0.1875
Outputs:
- mixed: bfloat16 [65536, 3584], P(('dp', 'expert'))
- grad_in: bfloat16 [64, 3584, 1024], P('expert', None, 'dp')
- grad_out: bfloat16 [64, 1024, 3584], P('expert', 'dp')
The draws below stay inside these ranges and needn't reach their ends.
Inputs may be any that keep to these rules, and one draw needn't show every extreme that they name: `expert_ids`: among the 256 tokens of one device, no expert is named by more than 6 routes; some expert is named exactly 6 times. pair_flags[j] equals pair_flags[j XOR (32)].
All inputs are finite; a program needn't handle non-finite values.
Results may differ from the reference program's by a relative error of at most 0.015.
Values may be sent and summed in bfloat16 or wider, within the bound.
No kernel may reach another device: no remote copies, remote signals or barrier semaphores. Data moves between devices by JAX's collectives and lax.ppermute only.
A program may use at most 192 MiB of HBM per device.

```python
import math
import jax
import jax.numpy as jnp
import numpy as np
from jax import lax

D = 3584
H = 1024
TOK_DEV = 256
TOP = 1
EXPERTS = 64
C = 6
TOKENS = 65536
N_DP = 4


def draw_pair_flags(key, part):
    half_count = EXPERTS // 2
    key_bits = jax.random.fold_in(key, 11)
    key_one = jax.random.fold_in(key, 12)
    key_gap = jax.random.fold_in(key, 13)
    base = jax.random.randint(key_bits, (half_count,), 0, 2, dtype=jnp.int32)
    first_lane = jax.random.randint(key_one, (), 0, half_count, dtype=jnp.int32)
    gap_lane = jax.random.randint(key_gap, (), 1, half_count, dtype=jnp.int32)
    second_lane = ((first_lane + gap_lane) % half_count).astype(jnp.int32)
    lanes = jnp.arange(half_count, dtype=jnp.int32)
    base = jnp.where(lanes == first_lane, 1, jnp.where(lanes == second_lane, 0, base)).astype(jnp.int32)
    return jnp.concatenate([base, base]).astype(jnp.int32)


def levels(own_key, dims, split, least, largest):
    factor_of, own = 1.0, jax.random.fold_in(own_key, 6)
    for axis_at, blocks in split:
        heights = jnp.exp(jax.random.uniform(jax.random.fold_in(own, axis_at), (blocks,), jnp.float32, least / len(split), largest / len(split)))
        factor_of = factor_of * jnp.repeat(heights, dims[axis_at] // blocks).reshape([-1 if axis == axis_at else 1 for axis in range(len(dims))])
    return factor_of


def assign_block(key, own, number, rows, amount, top, most, slope):
    ranking = jax.random.permutation(key, amount)
    heavy_load, usual = load_shares(amount, rows * top, most, slope, True), load_shares(amount, rows * top, most, slope, False)
    places = jnp.arange(amount)

    def named(lengths, rotation):
        used = int((lengths > 0).sum())
        fixed = max(1, used // 4)
        passed = fixed + (places - fixed + rotation * (used - fixed)) % max(1, amount - fixed)
        return jnp.zeros((amount,), jnp.int32).at[ranking[jnp.where(places < fixed, places, passed)]].set(jnp.asarray(lengths, jnp.int32))

    lengths = jnp.where(number % 4 == 0, named(heavy_load, number // 4), named(usual, number - number // 4 - 1))
    mixed = jax.random.permutation(jax.random.fold_in(own, 3), amount)
    giver, sink = mixed[0:amount // 2 * 2:2], mixed[1:amount // 2 * 2:2]
    slack = jnp.minimum(lengths[giver] - 1, most - lengths[sink]) // 2
    slack = jnp.where((giver == ranking[0]) | (sink == ranking[0]) | (lengths[sink] == 0), 0, jnp.maximum(slack, 0))
    passed = jax.random.randint(jax.random.fold_in(own, 4), (amount // 2,), 0, 1 << 20) % (slack + 1)
    lengths = lengths.at[giver].add(-passed).at[sink].add(passed)
    members = jnp.searchsorted(jnp.cumsum(lengths), jnp.arange(rows * top), side="right").astype(jnp.int32)
    listing = members.reshape(top, rows).T
    listing = listing[jax.random.permutation(jax.random.fold_in(own, 1), rows)]
    rotation = jax.random.randint(jax.random.fold_in(own, 2), (rows, 1), 0, top)
    return jnp.take_along_axis(listing, (jnp.arange(top)[None, :] + rotation) % top, axis=1)


def load_shares(count, total, bound, skew, full):
    weights = [(1 << 20) // math.isqrt(grade ** skew) + 1 for grade in range(1, count + 1)]
    largest = bound if full else min(bound, max(-(-total // count), total * weights[0] // sum(weights)))
    least = 1 if total - largest >= count - 1 else 0
    holding, spare = [largest] + [least] * (count - 1), total - largest - least * (count - 1)
    while spare > 0:
        free = [i for i in range(1, count) if holding[i] < largest] or [i for i in range(1, count) if holding[i] < bound]
        whole, left = sum([weights[i] for i in free]), spare
        for i in free:
            extra = min(bound - holding[i], max(1, left * weights[i] // whole), spare)
            holding[i] = holding[i] + extra
            spare = spare - extra
    return np.array(holding)


def bell_draw(stream_key, extent, width, most, shards=(), held_as=jnp.bfloat16):
    result = width * jax.random.normal(stream_key, extent, jnp.float32)
    if shards:
        result = result * levels(stream_key, extent, shards, -0.22, 0.18)
    return jnp.clip(result, -most, most).astype(held_as)


def setup_inputs(seed: int = 0) -> dict:
    keys = jax.random.split(jax.random.key(seed), 8)
    tokens = bell_draw(keys[0], (TOKENS, D), 1.0, 6.0, ((0, 256),))
    cotangent = bell_draw(keys[1], (TOKENS, D), 0.1, 0.59765625, ((0, 256),))
    expert_ids_keys = jax.random.split(jax.random.fold_in(keys[2], 1), TOKENS // TOK_DEV)
    expert_ids_turns = jax.random.permutation(jax.random.fold_in(keys[2], 3), TOKENS // TOK_DEV)
    expert_ids = jax.vmap(lambda own, number: assign_block(jax.random.fold_in(keys[2], 2), own, number, TOK_DEV, EXPERTS, TOP, C, 2))(expert_ids_keys, expert_ids_turns).reshape((TOKENS, TOP))
    gates = jnp.clip(0.2 + 0.8 * jax.random.uniform(keys[3], (TOKENS, TOP), jnp.float32) ** levels(keys[3], (TOKENS, TOP), ((0, 256),), -0.2, 0.2), 0.2, 1.0)
    pair_flags = draw_pair_flags(jax.random.fold_in(keys[7], 71), 0)
    w_in = bell_draw(keys[5], (EXPERTS, D, H), D ** -0.5, 0.09375, ((0, 64), (2, 4)))
    w_out = bell_draw(keys[6], (EXPERTS, H, D), H ** -0.5, 0.1875, ((0, 64), (1, 4)))
    return dict(tokens=tokens, cotangent=cotangent, expert_ids=expert_ids, gates=gates, pair_flags=pair_flags, w_in=w_in, w_out=w_out)


def reference(tokens, cotangent, expert_ids, gates, pair_flags, w_in, w_out):
    routed_count = TOKENS * TOP
    ids = expert_ids.reshape(-1).astype(jnp.int32)
    token_of = (jnp.arange(routed_count) // TOP).astype(jnp.int32)
    replica = (token_of // (TOK_DEV * EXPERTS)).astype(jnp.int32)
    weight = gates.reshape(-1)
    scaled = (weight[:, None] * cotangent[token_of].astype(jnp.float32)).astype(jnp.bfloat16)
    scaled_ext = jnp.concatenate([scaled, jnp.zeros((1, D), jnp.bfloat16)], axis=0)
    tokens_ext = jnp.concatenate([tokens, jnp.zeros((1, D), jnp.bfloat16)], axis=0)
    token_ext = jnp.concatenate([token_of, jnp.full((1,), TOKENS, jnp.int32)]).astype(jnp.int32)
    group = (ids * N_DP + replica).astype(jnp.int32)
    order = jnp.argsort(group, stable=True).astype(jnp.int32)
    counts = jnp.sum((group[:, None] == jnp.arange(EXPERTS * N_DP, dtype=jnp.int32)[None, :]).astype(jnp.int32), axis=0).astype(jnp.int32)
    starts = (jnp.cumsum(counts) - counts).astype(jnp.int32)
    span = EXPERTS * C
    order_ext = jnp.concatenate([order, jnp.full((span,), routed_count, jnp.int32)]).astype(jnp.int32)
    lanes = jnp.arange(span, dtype=jnp.int32)

    def step(carry, expert):
        win = w_in[expert]
        wout = w_out[expert]
        sum_in = jnp.zeros((D, H), jnp.float32)
        sum_out = jnp.zeros((H, D), jnp.float32)
        for rep in range(N_DP):
            slot = expert * N_DP + rep
            index = lax.dynamic_slice_in_dim(order_ext, starts[slot], span)
            index = jnp.where(lanes < counts[slot], index, routed_count).astype(jnp.int32)
            xrows = tokens_ext[token_ext[index]]
            drows = scaled_ext[index]
            pre = jnp.dot(xrows, win, preferred_element_type=jnp.float32)
            sig = jax.nn.sigmoid(pre)
            hidden = (pre * sig).astype(jnp.bfloat16)
            out_rows = jnp.dot(hidden, wout, preferred_element_type=jnp.float32).astype(jnp.bfloat16)
            carry = carry.at[index].set(out_rows, mode="drop")
            dhid = jnp.dot(drows, wout.T, preferred_element_type=jnp.float32)
            dpre = (dhid * sig * (1.0 + pre * (1.0 - sig))).astype(jnp.bfloat16)
            part_out = lax.optimization_barrier(jnp.dot(hidden.T, drows, preferred_element_type=jnp.float32).astype(jnp.bfloat16))
            part_in = lax.optimization_barrier(jnp.dot(xrows.T, dpre, preferred_element_type=jnp.float32).astype(jnp.bfloat16))
            sum_out = sum_out + part_out.astype(jnp.float32)
            sum_in = sum_in + part_in.astype(jnp.float32)
        return carry, (sum_in.astype(jnp.bfloat16), sum_out.astype(jnp.bfloat16))

    outs, grads = lax.scan(step, jnp.zeros((routed_count, D), jnp.bfloat16), jnp.arange(EXPERTS, dtype=jnp.int32))
    full_in, full_out = grads
    mixed = jnp.sum(weight.reshape(TOKENS, TOP, 1) * outs.reshape(TOKENS, TOP, D).astype(jnp.float32), axis=1).astype(jnp.bfloat16)
    partner = jnp.bitwise_xor(jnp.arange(EXPERTS, dtype=jnp.int32), (EXPERTS // 2) * pair_flags).astype(jnp.int32)
    return mixed, full_in[partner], full_out[partner]
```

```python
import jax
import jax.numpy as jnp
from jax import lax
from jax.sharding import Mesh, PartitionSpec as P


def partner_2(block, axis, distance):
    count = lax.axis_size(axis)
    route = []
    for low in range(count):
        high = low | 1 << distance
        if high != low and high < count:
            route += [(low, high), (high, low)]
    return lax.ppermute(block, axis, route)


def swap_core(block):
    return lax.ppermute(block, "dc", [(0, 1), (1, 0)])


def body(tokens, cotangent, expert_ids, gates, pair_flags, w_in, w_out):
    expert_count = lax.axis_size("expert")
    own_index = lax.axis_index("expert")
    half_axis = expert_count // 2
    pair_bit = half_axis.bit_length() - 1
    local_tokens, top_count = expert_ids.shape
    width = tokens.shape[1]
    capacity = max(2, 3 * local_tokens * top_count // (2 * expert_count))
    route_count = local_tokens * top_count
    slots = expert_count * capacity
    lanes = jnp.arange(expert_count, dtype=jnp.int32)
    partner = jnp.bitwise_xor(lanes, half_axis * pair_flags)
    flagged = pair_flags[own_index] == 1

    quarter_in = w_in[0]
    quarter_out = w_out[0]
    their_in, their_out = partner_2((quarter_in, quarter_out), "expert", pair_bit)
    quarter_in = jnp.where(flagged, their_in, quarter_in)
    quarter_out = jnp.where(flagged, their_out, quarter_out)
    half_in = lax.all_gather(quarter_in, "dx", axis=1, tiled=True)
    half_out = lax.all_gather(quarter_out, "dx", axis=0, tiled=True)

    flat_ids = expert_ids.reshape(-1)
    target_of = partner[flat_ids]
    onehot = (target_of[:, None] == lanes[None, :]).astype(jnp.int32)
    position = jnp.sum(jnp.cumsum(onehot, axis=0) * onehot, axis=1) - 1
    slot_of = target_of * capacity + position
    select = (slot_of[None, :] == jnp.arange(slots, dtype=jnp.int32)[:, None]).astype(
        jnp.bfloat16
    )
    token_of = jnp.arange(route_count, dtype=jnp.int32) // top_count
    route_rows = tokens[token_of] if top_count > 1 else tokens
    route_cot = cotangent[token_of] if top_count > 1 else cotangent
    scaled = (gates.reshape(-1)[:, None] * route_cot.astype(jnp.float32)).astype(jnp.bfloat16)
    send_rows = jnp.dot(select, route_rows, preferred_element_type=jnp.float32).astype(
        jnp.bfloat16
    )
    send_grads = jnp.dot(select, scaled, preferred_element_type=jnp.float32).astype(
        jnp.bfloat16
    )
    send = jnp.stack(
        [send_rows.reshape(expert_count, capacity, width),
         send_grads.reshape(expert_count, capacity, width)],
        axis=1,
    )
    recv = lax.all_to_all(send, "expert", split_axis=0, concat_axis=0, tiled=True)
    other = swap_core(recv)

    contract_last = (((1,), (1,)), ((), ()))
    contract_first = (((0,), (0,)), ((), ()))

    def expert_pass(block):
        rows = block[:, 0].reshape(slots, width)
        grads = block[:, 1].reshape(slots, width)
        pre = jnp.dot(rows, half_in, preferred_element_type=jnp.float32)
        sig = jax.nn.sigmoid(pre)
        hidden = (pre * sig).astype(jnp.bfloat16)
        out = jnp.dot(hidden, half_out, preferred_element_type=jnp.float32)
        dhid = lax.dot_general(grads, half_out, contract_last, preferred_element_type=jnp.float32)
        dpre = (dhid * sig * (1.0 + pre * (1.0 - sig))).astype(jnp.bfloat16)
        term_in = lax.dot_general(rows, dpre, contract_first, preferred_element_type=jnp.float32)
        term_out = lax.dot_general(hidden, grads, contract_first, preferred_element_type=jnp.float32)
        return out, term_in, term_out

    out_other, in_other, outg_other = expert_pass(other)
    back = swap_core(out_other.astype(jnp.bfloat16))
    out_own, in_own, outg_own = expert_pass(recv)
    expert_out = (out_own + back.astype(jnp.float32)).astype(jnp.bfloat16)

    term_in = (in_own + in_other).astype(jnp.bfloat16)
    term_out = (outg_own + outg_other).astype(jnp.bfloat16)
    grad_quarter_in = lax.psum_scatter(term_in, "dx", scatter_dimension=1, tiled=True)
    grad_quarter_out = lax.psum_scatter(term_out, "dx", scatter_dimension=0, tiled=True)

    returned = lax.all_to_all(
        expert_out.reshape(expert_count, capacity, width), "expert",
        split_axis=0, concat_axis=0, tiled=True,
    ).reshape(slots, width)
    route_out = lax.dot_general(
        select, returned, contract_first, preferred_element_type=jnp.float32
    )
    weighted = gates.reshape(local_tokens, top_count, 1) * route_out.astype(
        jnp.bfloat16
    ).astype(jnp.float32).reshape(local_tokens, top_count, width)
    mixed = jnp.sum(weighted, axis=1).astype(jnp.bfloat16)
    return (mixed, grad_quarter_in[None], grad_quarter_out[None])


def solution(mesh):
    devices = mesh.devices
    dp_count = devices.shape[0]
    split = Mesh(
        devices.reshape(dp_count // 2, 2, devices.shape[1]), ("dx", "dc", "expert")
    )
    rows = P(("dx", "dc", "expert"), None)
    placed = (
        rows,
        rows,
        rows,
        rows,
        P(),
        P("expert", None, ("dx", "dc")),
        P("expert", ("dx", "dc"), None),
    )
    return jax.shard_map(
        body,
        mesh=split,
        in_specs=placed,
        out_specs=(rows, P("expert", None, ("dx", "dc")), P("expert", ("dx", "dc"), None)),
        check_vma=False,
    )
```

```python
import jax
import jax.numpy as jnp
from jax import lax
from jax.sharding import Mesh, PartitionSpec as P


def partner_2(block, axis, distance):
    count = lax.axis_size(axis)
    route = []
    for low in range(count):
        high = low | 1 << distance
        if high != low and high < count:
            route += [(low, high), (high, low)]
    return lax.ppermute(block, axis, route)


def swap_core(block):
    return lax.ppermute(block, "dc", [(0, 1), (1, 0)])


def body(tokens, cotangent, expert_ids, gates, pair_flags, w_in, w_out):
    expert_count = lax.axis_size("expert")
    own_index = lax.axis_index("expert")
    half_axis = expert_count // 2
    pair_bit = half_axis.bit_length() - 1
    local_tokens, top_count = expert_ids.shape
    width = tokens.shape[1]
    capacity = max(2, 3 * local_tokens * top_count // (2 * expert_count))
    route_count = local_tokens * top_count
    slots = expert_count * capacity
    lanes = jnp.arange(expert_count, dtype=jnp.int32)
    partner = jnp.bitwise_xor(lanes, half_axis * pair_flags)
    flagged = pair_flags[own_index] == 1

    quarter_in = w_in[0]
    quarter_out = w_out[0]
    size_in = quarter_in.size
    both = jnp.concatenate([quarter_in.reshape(-1), quarter_out.reshape(-1)])
    both = jnp.where(flagged, partner_2(both, "expert", pair_bit), both)
    quarter_in = both[:size_in].reshape(quarter_in.shape)
    quarter_out = both[size_in:].reshape(quarter_out.shape)
    half_in = lax.all_gather(quarter_in, "dx", axis=1, tiled=True)
    half_out = lax.all_gather(quarter_out, "dx", axis=0, tiled=True)

    flat_ids = expert_ids.reshape(-1)
    target_of = partner[flat_ids]
    onehot = (target_of[:, None] == lanes[None, :]).astype(jnp.int32)
    position = jnp.sum(jnp.cumsum(onehot, axis=0) * onehot, axis=1) - 1
    slot_of = target_of * capacity + position
    select = (slot_of[None, :] == jnp.arange(slots, dtype=jnp.int32)[:, None]).astype(
        jnp.bfloat16
    )
    token_of = jnp.arange(route_count, dtype=jnp.int32) // top_count
    route_rows = tokens[token_of] if top_count > 1 else tokens
    route_cot = cotangent[token_of] if top_count > 1 else cotangent
    scaled = (gates.reshape(-1)[:, None] * route_cot.astype(jnp.float32)).astype(jnp.bfloat16)
    payload = jnp.concatenate([route_rows, scaled], axis=1)
    send = jnp.dot(select, payload, preferred_element_type=jnp.float32).astype(jnp.bfloat16)
    recv = lax.all_to_all(
        send.reshape(expert_count, capacity, 2 * width), "expert",
        split_axis=0, concat_axis=0, tiled=True,
    ).reshape(slots, 2 * width)
    other = swap_core(recv)

    contract_last = (((1,), (1,)), ((), ()))
    contract_first = (((0,), (0,)), ((), ()))

    def expert_pass(block):
        rows = block[:, :width]
        grads = block[:, width:]
        pre = jnp.dot(rows, half_in, preferred_element_type=jnp.float32)
        sig = jax.nn.sigmoid(pre)
        hidden = (pre * sig).astype(jnp.bfloat16)
        out = jnp.dot(hidden, half_out, preferred_element_type=jnp.float32)
        dhid = lax.dot_general(grads, half_out, contract_last, preferred_element_type=jnp.float32)
        dpre = (dhid * sig * (1.0 + pre * (1.0 - sig))).astype(jnp.bfloat16)
        term_in = lax.dot_general(rows, dpre, contract_first, preferred_element_type=jnp.float32)
        term_out = lax.dot_general(hidden, grads, contract_first, preferred_element_type=jnp.float32)
        return out, term_in, term_out

    out_other, in_other, outg_other = expert_pass(other)
    back = swap_core(out_other.astype(jnp.bfloat16))
    out_own, in_own, outg_own = expert_pass(recv)
    expert_out = (out_own + back.astype(jnp.float32)).astype(jnp.bfloat16)

    term_in = (in_own + in_other).astype(jnp.bfloat16)
    term_out = (outg_own + outg_other).astype(jnp.bfloat16)
    grad_quarter_in = lax.psum_scatter(term_in, "dx", scatter_dimension=1, tiled=True)
    grad_quarter_out = lax.psum_scatter(term_out, "dx", scatter_dimension=0, tiled=True)

    returned = lax.all_to_all(
        expert_out.reshape(expert_count, capacity, width), "expert",
        split_axis=0, concat_axis=0, tiled=True,
    ).reshape(slots, width)
    route_out = lax.dot_general(
        select, returned, contract_first, preferred_element_type=jnp.float32
    )
    weighted = gates.reshape(local_tokens, top_count, 1) * route_out.astype(
        jnp.bfloat16
    ).astype(jnp.float32).reshape(local_tokens, top_count, width)
    mixed = jnp.sum(weighted, axis=1).astype(jnp.bfloat16)
    return (mixed, grad_quarter_in[None], grad_quarter_out[None])


def solution(mesh):
    devices = mesh.devices
    dp_count = devices.shape[0]
    split = Mesh(
        devices.reshape(dp_count // 2, 2, devices.shape[1]), ("dx", "dc", "expert")
    )
    rows = P(("dx", "dc", "expert"), None)
    placed = (
        rows,
        rows,
        rows,
        rows,
        P(),
        P("expert", None, ("dx", "dc")),
        P("expert", ("dx", "dc"), None),
    )
    return jax.shard_map(
        body,
        mesh=split,
        in_specs=placed,
        out_specs=(rows, P("expert", None, ("dx", "dc")), P("expert", ("dx", "dc"), None)),
        check_vma=False,
    )
```

```python
import jax
import jax.numpy as jnp
from jax import lax
from jax.sharding import Mesh, PartitionSpec as P


def partner_2(block, axis, distance):
    count = lax.axis_size(axis)
    route = []
    for low in range(count):
        high = low | 1 << distance
        if high != low and high < count:
            route += [(low, high), (high, low)]
    return lax.ppermute(block, axis, route)


def swap_core(block):
    return lax.ppermute(block, "dc", [(0, 1), (1, 0)])


def body(tokens, cotangent, expert_ids, gates, pair_flags, w_in, w_out):
    expert_count = lax.axis_size("expert")
    own_index = lax.axis_index("expert")
    half_axis = expert_count // 2
    pair_bit = half_axis.bit_length() - 1
    local_tokens, top_count = expert_ids.shape
    width = tokens.shape[1]
    capacity = max(2, 3 * local_tokens * top_count // (2 * expert_count))
    route_count = local_tokens * top_count
    slots = expert_count * capacity
    lanes = jnp.arange(expert_count, dtype=jnp.int32)
    flagged = pair_flags[own_index] == 1

    quarter_in = w_in[0]
    quarter_out = w_out[0]
    size_in = quarter_in.size
    both = jnp.concatenate([quarter_in.reshape(-1), quarter_out.reshape(-1)])
    both = lax.all_gather(both, "dx", axis=0, tiled=False)
    pair_count = both.shape[0]
    half_in = both[:, :size_in].reshape((pair_count,) + quarter_in.shape)
    half_in = jnp.moveaxis(half_in, 0, 1).reshape(quarter_in.shape[0], -1)
    half_out = both[:, size_in:].reshape(pair_count * quarter_out.shape[0], -1)

    flat_ids = expert_ids.reshape(-1)
    target_of = flat_ids
    onehot = (target_of[:, None] == lanes[None, :]).astype(jnp.int32)
    position = jnp.sum(jnp.cumsum(onehot, axis=0) * onehot, axis=1) - 1
    slot_of = target_of * capacity + position
    select = (slot_of[None, :] == jnp.arange(slots, dtype=jnp.int32)[:, None]).astype(
        jnp.bfloat16
    )
    token_of = jnp.arange(route_count, dtype=jnp.int32) // top_count
    route_rows = tokens[token_of] if top_count > 1 else tokens
    route_cot = cotangent[token_of] if top_count > 1 else cotangent
    scaled = (gates.reshape(-1)[:, None] * route_cot.astype(jnp.float32)).astype(jnp.bfloat16)
    payload = jnp.concatenate([route_rows, scaled], axis=1)
    send = jnp.dot(select, payload, preferred_element_type=jnp.float32).astype(jnp.bfloat16)
    recv = lax.all_to_all(
        send.reshape(expert_count, capacity, 2 * width), "expert",
        split_axis=0, concat_axis=0, tiled=True,
    ).reshape(slots, 2 * width)
    other = swap_core(recv)

    contract_last = (((1,), (1,)), ((), ()))
    contract_first = (((0,), (0,)), ((), ()))

    def expert_pass(block):
        rows = block[:, :width]
        grads = block[:, width:]
        pre = jnp.dot(rows, half_in, preferred_element_type=jnp.float32)
        sig = jax.nn.sigmoid(pre)
        hidden = (pre * sig).astype(jnp.bfloat16)
        out = jnp.dot(hidden, half_out, preferred_element_type=jnp.float32)
        dhid = lax.dot_general(grads, half_out, contract_last, preferred_element_type=jnp.float32)
        dpre = (dhid * sig * (1.0 + pre * (1.0 - sig))).astype(jnp.bfloat16)
        term_in = lax.dot_general(rows, dpre, contract_first, preferred_element_type=jnp.float32)
        term_out = lax.dot_general(hidden, grads, contract_first, preferred_element_type=jnp.float32)
        return out, term_in, term_out

    out_other, in_other, outg_other = expert_pass(other)
    back = swap_core(out_other.astype(jnp.bfloat16))
    out_own, in_own, outg_own = expert_pass(recv)
    expert_out = (out_own + back.astype(jnp.float32)).astype(jnp.bfloat16)

    term_in = (in_own + in_other).astype(jnp.bfloat16)
    term_out = (outg_own + outg_other).astype(jnp.bfloat16)
    grad_quarter_in = lax.psum_scatter(term_in, "dx", scatter_dimension=1, tiled=True)
    grad_quarter_out = lax.psum_scatter(term_out, "dx", scatter_dimension=0, tiled=True)
    their_in, their_out = partner_2((grad_quarter_in, grad_quarter_out), "expert", pair_bit)
    grad_quarter_in = jnp.where(flagged, their_in, grad_quarter_in)
    grad_quarter_out = jnp.where(flagged, their_out, grad_quarter_out)

    returned = lax.all_to_all(
        expert_out.reshape(expert_count, capacity, width), "expert",
        split_axis=0, concat_axis=0, tiled=True,
    ).reshape(slots, width)
    route_out = lax.dot_general(
        select, returned, contract_first, preferred_element_type=jnp.float32
    )
    weighted = gates.reshape(local_tokens, top_count, 1) * route_out.astype(
        jnp.bfloat16
    ).astype(jnp.float32).reshape(local_tokens, top_count, width)
    mixed = jnp.sum(weighted, axis=1).astype(jnp.bfloat16)
    return (mixed, grad_quarter_in[None], grad_quarter_out[None])


def solution(mesh):
    devices = mesh.devices
    dp_count = devices.shape[0]
    split = Mesh(
        devices.reshape(dp_count // 2, 2, devices.shape[1]), ("dx", "dc", "expert")
    )
    rows = P(("dx", "dc", "expert"), None)
    placed = (
        rows,
        rows,
        rows,
        rows,
        P(),
        P("expert", None, ("dx", "dc")),
        P("expert", ("dx", "dc"), None),
    )
    return jax.shard_map(
        body,
        mesh=split,
        in_specs=placed,
        out_specs=(rows, P("expert", None, ("dx", "dc")), P("expert", ("dx", "dc"), None)),
        check_vma=False,
    )
```

```python
import jax
import jax.numpy as jnp
from jax import lax
from jax.sharding import Mesh, PartitionSpec as P


def partner_2(block, axis, distance):
    count = lax.axis_size(axis)
    route = []
    for low in range(count):
        high = low | 1 << distance
        if high != low and high < count:
            route += [(low, high), (high, low)]
    return lax.ppermute(block, axis, route)


def swap_core(block):
    return lax.ppermute(block, "dc", [(0, 1), (1, 0)])


def body(tokens, cotangent, expert_ids, gates, pair_flags, w_in, w_out):
    expert_count = lax.axis_size("expert")
    own_index = lax.axis_index("expert")
    half_axis = expert_count // 2
    pair_bit = half_axis.bit_length() - 1
    local_tokens, top_count = expert_ids.shape
    width = tokens.shape[1]
    capacity = max(2, 3 * local_tokens * top_count // (2 * expert_count))
    route_count = local_tokens * top_count
    slots = expert_count * capacity
    lanes = jnp.arange(expert_count, dtype=jnp.int32)
    partner = jnp.bitwise_xor(lanes, half_axis * pair_flags)
    flagged = pair_flags[own_index] == 1

    quarter_in = w_in[0].T
    quarter_out = w_out[0]
    their_in, their_out = partner_2((quarter_in, quarter_out), "expert", pair_bit)
    quarter_in = jnp.where(flagged, their_in, quarter_in)
    quarter_out = jnp.where(flagged, their_out, quarter_out)
    halves = lax.all_gather(jnp.stack([quarter_in, quarter_out]), "dx", axis=1, tiled=True)
    half_in = halves[0]
    half_out = halves[1]

    flat_ids = expert_ids.reshape(-1)
    target_of = partner[flat_ids]
    onehot = (target_of[:, None] == lanes[None, :]).astype(jnp.int32)
    position = jnp.sum(jnp.cumsum(onehot, axis=0) * onehot, axis=1) - 1
    slot_of = target_of * capacity + position
    select = (slot_of[None, :] == jnp.arange(slots, dtype=jnp.int32)[:, None]).astype(
        jnp.bfloat16
    )
    token_of = jnp.arange(route_count, dtype=jnp.int32) // top_count
    route_rows = tokens[token_of] if top_count > 1 else tokens
    route_cot = cotangent[token_of] if top_count > 1 else cotangent
    scaled = (gates.reshape(-1)[:, None] * route_cot.astype(jnp.float32)).astype(jnp.bfloat16)
    payload = jnp.concatenate([route_rows, scaled], axis=1)
    send = jnp.dot(select, payload, preferred_element_type=jnp.float32).astype(jnp.bfloat16)
    recv = lax.all_to_all(
        send.reshape(expert_count, capacity, 2 * width), "expert",
        split_axis=0, concat_axis=0, tiled=True,
    ).reshape(slots, 2 * width)
    other = swap_core(recv)

    contract_last = (((1,), (1,)), ((), ()))
    contract_first = (((0,), (0,)), ((), ()))

    def expert_pass(block):
        rows = block[:, :width]
        grads = block[:, width:]
        pre = lax.dot_general(rows, half_in, contract_last, preferred_element_type=jnp.float32)
        sig = jax.nn.sigmoid(pre)
        hidden = (pre * sig).astype(jnp.bfloat16)
        out = jnp.dot(hidden, half_out, preferred_element_type=jnp.float32)
        dhid = lax.dot_general(grads, half_out, contract_last, preferred_element_type=jnp.float32)
        dpre = (dhid * sig * (1.0 + pre * (1.0 - sig))).astype(jnp.bfloat16)
        term_in = lax.dot_general(dpre, rows, contract_first, preferred_element_type=jnp.float32)
        term_out = lax.dot_general(hidden, grads, contract_first, preferred_element_type=jnp.float32)
        return out, term_in, term_out

    out_other, in_other, outg_other = expert_pass(other)
    back = swap_core(out_other.astype(jnp.bfloat16))
    out_own, in_own, outg_own = expert_pass(recv)
    expert_out = (out_own + back.astype(jnp.float32)).astype(jnp.bfloat16)

    terms = jnp.stack([in_own + in_other, outg_own + outg_other]).astype(jnp.bfloat16)
    grad_quarters = lax.psum_scatter(terms, "dx", scatter_dimension=1, tiled=True)
    grad_quarter_in = grad_quarters[0].T
    grad_quarter_out = grad_quarters[1]

    returned = lax.all_to_all(
        expert_out.reshape(expert_count, capacity, width), "expert",
        split_axis=0, concat_axis=0, tiled=True,
    ).reshape(slots, width)
    route_out = lax.dot_general(
        select, returned, contract_first, preferred_element_type=jnp.float32
    )
    weighted = gates.reshape(local_tokens, top_count, 1) * route_out.astype(
        jnp.bfloat16
    ).astype(jnp.float32).reshape(local_tokens, top_count, width)
    mixed = jnp.sum(weighted, axis=1).astype(jnp.bfloat16)
    return (mixed, grad_quarter_in[None], grad_quarter_out[None])


def solution(mesh):
    devices = mesh.devices
    dp_count = devices.shape[0]
    split = Mesh(
        devices.reshape(dp_count // 2, 2, devices.shape[1]), ("dx", "dc", "expert")
    )
    rows = P(("dx", "dc", "expert"), None)
    placed = (
        rows,
        rows,
        rows,
        rows,
        P(),
        P("expert", None, ("dx", "dc")),
        P("expert", ("dx", "dc"), None),
    )
    return jax.shard_map(
        body,
        mesh=split,
        in_specs=placed,
        out_specs=(rows, P("expert", None, ("dx", "dc")), P("expert", ("dx", "dc"), None)),
        check_vma=False,
    )
```

```python
import jax
import jax.numpy as jnp
from jax import lax
from jax.sharding import Mesh, PartitionSpec as P


def partner_2(block, axis, distance):
    count = lax.axis_size(axis)
    route = []
    for low in range(count):
        high = low | 1 << distance
        if high != low and high < count:
            route += [(low, high), (high, low)]
    return lax.ppermute(block, axis, route)


def swap_core(block):
    return lax.ppermute(block, "dc", [(0, 1), (1, 0)])


def body(tokens, cotangent, expert_ids, gates, pair_flags, w_in, w_out):
    expert_count = lax.axis_size("expert")
    own_index = lax.axis_index("expert")
    half_axis = expert_count // 2
    pair_bit = half_axis.bit_length() - 1
    local_tokens, top_count = expert_ids.shape
    width = tokens.shape[1]
    capacity = max(2, 3 * local_tokens * top_count // (2 * expert_count))
    route_count = local_tokens * top_count
    slots = expert_count * capacity
    lanes = jnp.arange(expert_count, dtype=jnp.int32)
    flagged = pair_flags[own_index] == 1

    halves = lax.all_gather(jnp.stack([w_in[0].T, w_out[0]]), "dx", axis=1, tiled=True)
    half_in = halves[0]
    half_out = halves[1]

    flat_ids = expert_ids.reshape(-1)
    target_of = flat_ids
    onehot = (target_of[:, None] == lanes[None, :]).astype(jnp.int32)
    position = jnp.sum(jnp.cumsum(onehot, axis=0) * onehot, axis=1) - 1
    slot_of = target_of * capacity + position
    select = (slot_of[None, :] == jnp.arange(slots, dtype=jnp.int32)[:, None]).astype(
        jnp.bfloat16
    )
    token_of = jnp.arange(route_count, dtype=jnp.int32) // top_count
    route_rows = tokens[token_of] if top_count > 1 else tokens
    route_cot = cotangent[token_of] if top_count > 1 else cotangent
    scaled = (gates.reshape(-1)[:, None] * route_cot.astype(jnp.float32)).astype(jnp.bfloat16)
    payload = jnp.concatenate([route_rows, scaled], axis=1)
    send = jnp.dot(select, payload, preferred_element_type=jnp.float32).astype(jnp.bfloat16)
    recv = lax.all_to_all(
        send.reshape(expert_count, capacity, 2 * width), "expert",
        split_axis=0, concat_axis=0, tiled=True,
    ).reshape(slots, 2 * width)
    other = swap_core(recv)

    contract_last = (((1,), (1,)), ((), ()))
    contract_first = (((0,), (0,)), ((), ()))

    def expert_pass(block):
        rows = block[:, :width]
        grads = block[:, width:]
        pre = lax.dot_general(rows, half_in, contract_last, preferred_element_type=jnp.float32)
        sig = jax.nn.sigmoid(pre)
        hidden = (pre * sig).astype(jnp.bfloat16)
        out = jnp.dot(hidden, half_out, preferred_element_type=jnp.float32)
        dhid = lax.dot_general(grads, half_out, contract_last, preferred_element_type=jnp.float32)
        dpre = (dhid * sig * (1.0 + pre * (1.0 - sig))).astype(jnp.bfloat16)
        term_in = lax.dot_general(dpre, rows, contract_first, preferred_element_type=jnp.float32)
        term_out = lax.dot_general(hidden, grads, contract_first, preferred_element_type=jnp.float32)
        return out, term_in, term_out

    out_other, in_other, outg_other = expert_pass(other)
    back = swap_core(out_other.astype(jnp.bfloat16))
    out_own, in_own, outg_own = expert_pass(recv)
    expert_out = (out_own + back.astype(jnp.float32)).astype(jnp.bfloat16)

    term_out = (outg_own + outg_other).astype(jnp.bfloat16)
    term_in = (in_own + in_other).astype(jnp.bfloat16)
    quarter_out = lax.psum_scatter(term_out, "dx", scatter_dimension=0, tiled=True)
    quarter_in = lax.psum_scatter(term_in, "dx", scatter_dimension=0, tiled=True)

    returned = lax.all_to_all(
        expert_out.reshape(expert_count, capacity, width), "expert",
        split_axis=0, concat_axis=0, tiled=True,
    ).reshape(slots, width)
    route_out = lax.dot_general(
        select, returned, contract_first, preferred_element_type=jnp.float32
    )
    weighted = gates.reshape(local_tokens, top_count, 1) * route_out.astype(
        jnp.bfloat16
    ).astype(jnp.float32).reshape(local_tokens, top_count, width)
    mixed = jnp.sum(weighted, axis=1).astype(jnp.bfloat16)

    quarters, _ = lax.optimization_barrier((jnp.stack([quarter_in, quarter_out]), returned))
    quarters = jnp.where(flagged, partner_2(quarters, "expert", pair_bit), quarters)
    return (mixed, quarters[0].T[None], quarters[1][None])


def solution(mesh):
    devices = mesh.devices
    dp_count = devices.shape[0]
    split = Mesh(
        devices.reshape(dp_count // 2, 2, devices.shape[1]), ("dx", "dc", "expert")
    )
    rows = P(("dx", "dc", "expert"), None)
    placed = (
        rows,
        rows,
        rows,
        rows,
        P(),
        P("expert", None, ("dx", "dc")),
        P("expert", ("dx", "dc"), None),
    )
    return jax.shard_map(
        body,
        mesh=split,
        in_specs=placed,
        out_specs=(rows, P("expert", None, ("dx", "dc")), P("expert", ("dx", "dc"), None)),
        check_vma=False,
    )
```

```python
import jax
import jax.numpy as jnp
from jax import lax
from jax.sharding import Mesh, PartitionSpec as P


def partner_2(block, axis, distance):
    count = lax.axis_size(axis)
    route = []
    for low in range(count):
        high = low | 1 << distance
        if high != low and high < count:
            route += [(low, high), (high, low)]
    return lax.ppermute(block, axis, route)


def swap_core(block):
    return lax.ppermute(block, "dc", [(0, 1), (1, 0)])


def body(tokens, cotangent, expert_ids, gates, pair_flags, w_in, w_out):
    expert_count = lax.axis_size("expert")
    own_index = lax.axis_index("expert")
    half_axis = expert_count // 2
    pair_bit = half_axis.bit_length() - 1
    local_tokens, top_count = expert_ids.shape
    width = tokens.shape[1]
    capacity = max(2, 3 * local_tokens * top_count // (2 * expert_count))
    route_count = local_tokens * top_count
    slots = expert_count * capacity
    lanes = jnp.arange(expert_count, dtype=jnp.int32)
    partner = jnp.bitwise_xor(lanes, half_axis * pair_flags)
    flagged = pair_flags[own_index] == 1

    quarter_in = w_in[0]
    quarter_out = w_out[0]

    flat_ids = expert_ids.reshape(-1)
    target_of = partner[flat_ids]
    onehot = (target_of[:, None] == lanes[None, :]).astype(jnp.int32)
    position = jnp.sum(jnp.cumsum(onehot, axis=0) * onehot, axis=1) - 1
    slot_of = target_of * capacity + position
    select = (slot_of[None, :] == jnp.arange(slots, dtype=jnp.int32)[:, None]).astype(
        jnp.bfloat16
    )
    token_of = jnp.arange(route_count, dtype=jnp.int32) // top_count
    route_rows = tokens[token_of] if top_count > 1 else tokens
    route_cot = cotangent[token_of] if top_count > 1 else cotangent
    scaled = (gates.reshape(-1)[:, None] * route_cot.astype(jnp.float32)).astype(jnp.bfloat16)
    payload = jnp.concatenate([route_rows, scaled], axis=1)
    send = jnp.dot(select, payload, preferred_element_type=jnp.float32).astype(jnp.bfloat16)
    their_in, send_kept = lax.optimization_barrier((quarter_in, send))
    quarter_in = jnp.where(flagged, partner_2(their_in, "expert", pair_bit), quarter_in)
    half_in = lax.all_gather(quarter_in, "dx", axis=1, tiled=True)
    recv = lax.all_to_all(
        send_kept.reshape(expert_count, capacity, 2 * width), "expert",
        split_axis=0, concat_axis=0, tiled=True,
    ).reshape(slots, 2 * width)
    their_out, recv = lax.optimization_barrier((quarter_out, recv))
    quarter_out = jnp.where(flagged, partner_2(their_out, "expert", pair_bit), quarter_out)
    half_out = lax.all_gather(quarter_out, "dx", axis=0, tiled=True)
    other = swap_core(recv)

    contract_last = (((1,), (1,)), ((), ()))
    contract_first = (((0,), (0,)), ((), ()))

    def expert_pass(block):
        rows = block[:, :width]
        grads = block[:, width:]
        pre = jnp.dot(rows, half_in, preferred_element_type=jnp.float32)
        sig = jax.nn.sigmoid(pre)
        hidden = (pre * sig).astype(jnp.bfloat16)
        out = jnp.dot(hidden, half_out, preferred_element_type=jnp.float32)
        dhid = lax.dot_general(grads, half_out, contract_last, preferred_element_type=jnp.float32)
        dpre = (dhid * sig * (1.0 + pre * (1.0 - sig))).astype(jnp.bfloat16)
        term_in = lax.dot_general(rows, dpre, contract_first, preferred_element_type=jnp.float32)
        term_out = lax.dot_general(hidden, grads, contract_first, preferred_element_type=jnp.float32)
        return out, term_in, term_out

    out_other, in_other, outg_other = expert_pass(other)
    back = swap_core(out_other.astype(jnp.bfloat16))
    out_own, in_own, outg_own = expert_pass(recv)
    expert_out = (out_own + back.astype(jnp.float32)).astype(jnp.bfloat16)

    term_in = (in_own + in_other).astype(jnp.bfloat16)
    term_out = (outg_own + outg_other).astype(jnp.bfloat16)
    grad_quarter_in = lax.psum_scatter(term_in, "dx", scatter_dimension=1, tiled=True)
    grad_quarter_out = lax.psum_scatter(term_out, "dx", scatter_dimension=0, tiled=True)

    returned = lax.all_to_all(
        expert_out.reshape(expert_count, capacity, width), "expert",
        split_axis=0, concat_axis=0, tiled=True,
    ).reshape(slots, width)
    route_out = lax.dot_general(
        select, returned, contract_first, preferred_element_type=jnp.float32
    )
    weighted = gates.reshape(local_tokens, top_count, 1) * route_out.astype(
        jnp.bfloat16
    ).astype(jnp.float32).reshape(local_tokens, top_count, width)
    mixed = jnp.sum(weighted, axis=1).astype(jnp.bfloat16)
    return (mixed, grad_quarter_in[None], grad_quarter_out[None])


def solution(mesh):
    devices = mesh.devices
    dp_count = devices.shape[0]
    split = Mesh(
        devices.reshape(dp_count // 2, 2, devices.shape[1]), ("dx", "dc", "expert")
    )
    rows = P(("dx", "dc", "expert"), None)
    placed = (
        rows,
        rows,
        rows,
        rows,
        P(),
        P("expert", None, ("dx", "dc")),
        P("expert", ("dx", "dc"), None),
    )
    return jax.shard_map(
        body,
        mesh=split,
        in_specs=placed,
        out_specs=(rows, P("expert", None, ("dx", "dc")), P("expert", ("dx", "dc"), None)),
        check_vma=False,
    )
```

```python
import jax
import jax.numpy as jnp
from jax import lax
from jax.sharding import Mesh, PartitionSpec as P


def swap_core(block):
    return lax.ppermute(block, "dc", [(0, 1), (1, 0)])


EXPERT = ("zh", "er")


def body(tokens, cotangent, expert_ids, gates, pair_flags, w_in, w_out):
    half_axis = lax.axis_size("er")
    expert_count = 2 * half_axis
    high = lax.axis_index("zh")
    own_index = high * half_axis + lax.axis_index("er")
    local_tokens, top_count = expert_ids.shape
    width = tokens.shape[1]
    capacity = max(2, 3 * local_tokens * top_count // (2 * expert_count))
    route_count = local_tokens * top_count
    slots = expert_count * capacity
    lanes = jnp.arange(expert_count, dtype=jnp.int32)
    partner = jnp.bitwise_xor(lanes, half_axis * pair_flags)
    flagged = pair_flags[own_index] == 1

    quarter_in = w_in[0]
    quarter_out = w_out[0]
    pair_in, pair_out = lax.all_gather((quarter_in, quarter_out), "zh", axis=0, tiled=False)
    pick = jnp.where(flagged, 1 - high, high)
    quarter_in = jnp.where(pick == 0, pair_in[0], pair_in[1])
    quarter_out = jnp.where(pick == 0, pair_out[0], pair_out[1])
    half_in = lax.all_gather(quarter_in, "dx", axis=1, tiled=True)
    half_out = lax.all_gather(quarter_out, "dx", axis=0, tiled=True)

    flat_ids = expert_ids.reshape(-1)
    target_of = partner[flat_ids]
    onehot = (target_of[:, None] == lanes[None, :]).astype(jnp.int32)
    position = jnp.sum(jnp.cumsum(onehot, axis=0) * onehot, axis=1) - 1
    slot_of = target_of * capacity + position
    select = (slot_of[None, :] == jnp.arange(slots, dtype=jnp.int32)[:, None]).astype(
        jnp.bfloat16
    )
    token_of = jnp.arange(route_count, dtype=jnp.int32) // top_count
    route_rows = tokens[token_of] if top_count > 1 else tokens
    route_cot = cotangent[token_of] if top_count > 1 else cotangent
    scaled = (gates.reshape(-1)[:, None] * route_cot.astype(jnp.float32)).astype(jnp.bfloat16)
    payload = jnp.concatenate([route_rows, scaled], axis=1)
    send = jnp.dot(select, payload, preferred_element_type=jnp.float32).astype(jnp.bfloat16)
    recv = lax.all_to_all(
        send.reshape(expert_count, capacity, 2 * width), EXPERT,
        split_axis=0, concat_axis=0, tiled=True,
    ).reshape(slots, 2 * width)
    other = swap_core(recv)

    contract_last = (((1,), (1,)), ((), ()))
    contract_first = (((0,), (0,)), ((), ()))

    def expert_pass(block):
        rows = block[:, :width]
        grads = block[:, width:]
        pre = jnp.dot(rows, half_in, preferred_element_type=jnp.float32)
        sig = jax.nn.sigmoid(pre)
        hidden = (pre * sig).astype(jnp.bfloat16)
        out = jnp.dot(hidden, half_out, preferred_element_type=jnp.float32)
        dhid = lax.dot_general(grads, half_out, contract_last, preferred_element_type=jnp.float32)
        dpre = (dhid * sig * (1.0 + pre * (1.0 - sig))).astype(jnp.bfloat16)
        term_in = lax.dot_general(rows, dpre, contract_first, preferred_element_type=jnp.float32)
        term_out = lax.dot_general(hidden, grads, contract_first, preferred_element_type=jnp.float32)
        return out, term_in, term_out

    out_other, in_other, outg_other = expert_pass(other)
    back = swap_core(out_other.astype(jnp.bfloat16))
    out_own, in_own, outg_own = expert_pass(recv)
    expert_out = (out_own + back.astype(jnp.float32)).astype(jnp.bfloat16)

    term_in = (in_own + in_other).astype(jnp.bfloat16)
    term_out = (outg_own + outg_other).astype(jnp.bfloat16)
    grad_quarter_in = lax.psum_scatter(term_in, "dx", scatter_dimension=1, tiled=True)
    grad_quarter_out = lax.psum_scatter(term_out, "dx", scatter_dimension=0, tiled=True)

    returned = lax.all_to_all(
        expert_out.reshape(expert_count, capacity, width), EXPERT,
        split_axis=0, concat_axis=0, tiled=True,
    ).reshape(slots, width)
    route_out = lax.dot_general(
        select, returned, contract_first, preferred_element_type=jnp.float32
    )
    weighted = gates.reshape(local_tokens, top_count, 1) * route_out.astype(
        jnp.bfloat16
    ).astype(jnp.float32).reshape(local_tokens, top_count, width)
    mixed = jnp.sum(weighted, axis=1).astype(jnp.bfloat16)
    return (mixed, grad_quarter_in[None], grad_quarter_out[None])


def solution(mesh):
    devices = mesh.devices
    dp_count = devices.shape[0]
    split = Mesh(
        devices.reshape(dp_count // 2, 2, 2, devices.shape[1] // 2), ("dx", "dc") + EXPERT
    )
    rows = P(("dx", "dc") + EXPERT, None)
    placed = (
        rows,
        rows,
        rows,
        rows,
        P(),
        P(EXPERT, None, ("dx", "dc")),
        P(EXPERT, ("dx", "dc"), None),
    )
    return jax.shard_map(
        body,
        mesh=split,
        in_specs=placed,
        out_specs=(rows, P(EXPERT, None, ("dx", "dc")), P(EXPERT, ("dx", "dc"), None)),
        check_vma=False,
    )
```

```python
import jax
import jax.numpy as jnp
from jax import lax
from jax.sharding import Mesh, PartitionSpec as P


def partner_2(block, axis, distance):
    count = lax.axis_size(axis)
    route = []
    for low in range(count):
        high = low | 1 << distance
        if high != low and high < count:
            route += [(low, high), (high, low)]
    return lax.ppermute(block, axis, route)


def swap_core(block):
    return lax.ppermute(block, "dc", [(0, 1), (1, 0)])


def body(tokens, cotangent, expert_ids, gates, pair_flags, w_in, w_out):
    expert_count = lax.axis_size("expert")
    own_index = lax.axis_index("expert")
    half_axis = expert_count // 2
    pair_bit = half_axis.bit_length() - 1
    local_tokens, top_count = expert_ids.shape
    width = tokens.shape[1]
    capacity = max(2, 3 * local_tokens * top_count // (2 * expert_count))
    route_count = local_tokens * top_count
    slots = expert_count * capacity
    lanes = jnp.arange(expert_count, dtype=jnp.int32)
    partner = jnp.bitwise_xor(lanes, half_axis * pair_flags)
    flagged = pair_flags[own_index] == 1

    quarter_in = w_in[0].T
    quarter_out = w_out[0]
    their_in, their_out = partner_2((quarter_in, quarter_out), "expert", pair_bit)
    quarter_in = jnp.where(flagged, their_in, quarter_in)
    quarter_out = jnp.where(flagged, their_out, quarter_out)

    flat_ids = expert_ids.reshape(-1)
    target_of = partner[flat_ids]
    onehot = (target_of[:, None] == lanes[None, :]).astype(jnp.int32)
    position = jnp.sum(jnp.cumsum(onehot, axis=0) * onehot, axis=1) - 1
    slot_of = target_of * capacity + position
    select = (slot_of[None, :] == jnp.arange(slots, dtype=jnp.int32)[:, None]).astype(
        jnp.bfloat16
    )
    token_of = jnp.arange(route_count, dtype=jnp.int32) // top_count
    route_rows = tokens[token_of] if top_count > 1 else tokens
    route_cot = cotangent[token_of] if top_count > 1 else cotangent
    scaled = (gates.reshape(-1)[:, None] * route_cot.astype(jnp.float32)).astype(jnp.bfloat16)
    payload = jnp.concatenate([route_rows, scaled], axis=1)
    send = jnp.dot(select, payload, preferred_element_type=jnp.float32).astype(jnp.bfloat16)
    send, quarters = lax.optimization_barrier((send, jnp.stack([quarter_in, quarter_out])))
    halves = lax.all_gather(quarters, "dx", axis=1, tiled=True)
    half_in = halves[0]
    half_out = halves[1]
    recv = lax.all_to_all(
        send.reshape(expert_count, capacity, 2 * width), "expert",
        split_axis=0, concat_axis=0, tiled=True,
    ).reshape(slots, 2 * width)
    other = swap_core(recv)

    contract_last = (((1,), (1,)), ((), ()))
    contract_first = (((0,), (0,)), ((), ()))

    def expert_pass(block):
        rows = block[:, :width]
        grads = block[:, width:]
        pre = lax.dot_general(rows, half_in, contract_last, preferred_element_type=jnp.float32)
        sig = jax.nn.sigmoid(pre)
        hidden = (pre * sig).astype(jnp.bfloat16)
        out = jnp.dot(hidden, half_out, preferred_element_type=jnp.float32)
        dhid = lax.dot_general(grads, half_out, contract_last, preferred_element_type=jnp.float32)
        dpre = (dhid * sig * (1.0 + pre * (1.0 - sig))).astype(jnp.bfloat16)
        term_in = lax.dot_general(dpre, rows, contract_first, preferred_element_type=jnp.float32)
        term_out = lax.dot_general(hidden, grads, contract_first, preferred_element_type=jnp.float32)
        return out, term_in, term_out

    out_other, in_other, outg_other = expert_pass(other)
    back = swap_core(out_other.astype(jnp.bfloat16))
    out_own, in_own, outg_own = expert_pass(recv)
    expert_out = (out_own + back.astype(jnp.float32)).astype(jnp.bfloat16)

    terms = jnp.stack([in_own + in_other, outg_own + outg_other]).astype(jnp.bfloat16)
    grad_quarters = lax.psum_scatter(terms, "dx", scatter_dimension=1, tiled=True)
    grad_quarter_in = grad_quarters[0].T
    grad_quarter_out = grad_quarters[1]

    returned = lax.all_to_all(
        expert_out.reshape(expert_count, capacity, width), "expert",
        split_axis=0, concat_axis=0, tiled=True,
    ).reshape(slots, width)
    route_out = lax.dot_general(
        select, returned, contract_first, preferred_element_type=jnp.float32
    )
    weighted = gates.reshape(local_tokens, top_count, 1) * route_out.astype(
        jnp.bfloat16
    ).astype(jnp.float32).reshape(local_tokens, top_count, width)
    mixed = jnp.sum(weighted, axis=1).astype(jnp.bfloat16)
    return (mixed, grad_quarter_in[None], grad_quarter_out[None])


def solution(mesh):
    devices = mesh.devices
    dp_count = devices.shape[0]
    split = Mesh(
        devices.reshape(dp_count // 2, 2, devices.shape[1]), ("dx", "dc", "expert")
    )
    rows = P(("dx", "dc", "expert"), None)
    placed = (
        rows,
        rows,
        rows,
        rows,
        P(),
        P("expert", None, ("dx", "dc")),
        P("expert", ("dx", "dc"), None),
    )
    return jax.shard_map(
        body,
        mesh=split,
        in_specs=placed,
        out_specs=(rows, P("expert", None, ("dx", "dc")), P("expert", ("dx", "dc"), None)),
        check_vma=False,
    )
```

```python
import jax
import jax.numpy as jnp
from jax import lax
from jax.sharding import Mesh, PartitionSpec as P


def partner_2(block, axis, distance):
    count = lax.axis_size(axis)
    route = []
    for low in range(count):
        high = low | 1 << distance
        if high != low and high < count:
            route += [(low, high), (high, low)]
    return lax.ppermute(block, axis, route)


def swap_core(block):
    return lax.ppermute(block, "dc", [(0, 1), (1, 0)])


def body(tokens, cotangent, expert_ids, gates, pair_flags, w_in, w_out):
    expert_count = lax.axis_size("expert")
    own_index = lax.axis_index("expert")
    half_axis = expert_count // 2
    pair_bit = half_axis.bit_length() - 1
    local_tokens, top_count = expert_ids.shape
    width = tokens.shape[1]
    capacity = max(2, 3 * local_tokens * top_count // (2 * expert_count))
    route_count = local_tokens * top_count
    slots = expert_count * capacity
    lanes = jnp.arange(expert_count, dtype=jnp.int32)
    partner = jnp.bitwise_xor(lanes, half_axis * pair_flags)
    flagged = pair_flags[own_index] == 1

    quarter_in = w_in[0].T
    quarter_out = w_out[0]
    their_in = partner_2(quarter_in, "expert", pair_bit)
    their_in, quarter_out = lax.optimization_barrier((their_in, quarter_out))
    their_out = partner_2(quarter_out, "expert", pair_bit)
    quarter_in = jnp.where(flagged, their_in, quarter_in)
    quarter_out = jnp.where(flagged, their_out, quarter_out)

    flat_ids = expert_ids.reshape(-1)
    target_of = partner[flat_ids]
    onehot = (target_of[:, None] == lanes[None, :]).astype(jnp.int32)
    position = jnp.sum(jnp.cumsum(onehot, axis=0) * onehot, axis=1) - 1
    slot_of = target_of * capacity + position
    select = (slot_of[None, :] == jnp.arange(slots, dtype=jnp.int32)[:, None]).astype(
        jnp.bfloat16
    )
    token_of = jnp.arange(route_count, dtype=jnp.int32) // top_count
    route_rows = tokens[token_of] if top_count > 1 else tokens
    route_cot = cotangent[token_of] if top_count > 1 else cotangent
    scaled = (gates.reshape(-1)[:, None] * route_cot.astype(jnp.float32)).astype(jnp.bfloat16)
    payload = jnp.concatenate([route_rows, scaled], axis=1)
    send = jnp.dot(select, payload, preferred_element_type=jnp.float32).astype(jnp.bfloat16)
    send, quarters = lax.optimization_barrier((send, jnp.stack([quarter_in, quarter_out])))
    halves = lax.all_gather(quarters, "dx", axis=1, tiled=True)
    half_in = halves[0]
    half_out = halves[1]
    recv = lax.all_to_all(
        send.reshape(expert_count, capacity, 2 * width), "expert",
        split_axis=0, concat_axis=0, tiled=True,
    ).reshape(slots, 2 * width)
    other = swap_core(recv)

    contract_last = (((1,), (1,)), ((), ()))
    contract_first = (((0,), (0,)), ((), ()))

    def expert_pass(block):
        rows = block[:, :width]
        grads = block[:, width:]
        pre = lax.dot_general(rows, half_in, contract_last, preferred_element_type=jnp.float32)
        sig = jax.nn.sigmoid(pre)
        hidden = (pre * sig).astype(jnp.bfloat16)
        out = jnp.dot(hidden, half_out, preferred_element_type=jnp.float32)
        dhid = lax.dot_general(grads, half_out, contract_last, preferred_element_type=jnp.float32)
        dpre = (dhid * sig * (1.0 + pre * (1.0 - sig))).astype(jnp.bfloat16)
        term_in = lax.dot_general(dpre, rows, contract_first, preferred_element_type=jnp.float32)
        term_out = lax.dot_general(hidden, grads, contract_first, preferred_element_type=jnp.float32)
        return out, term_in, term_out

    out_other, in_other, outg_other = expert_pass(other)
    back = swap_core(out_other.astype(jnp.bfloat16))
    out_own, in_own, outg_own = expert_pass(recv)
    expert_out = (out_own + back.astype(jnp.float32)).astype(jnp.bfloat16)

    terms = jnp.stack([in_own + in_other, outg_own + outg_other]).astype(jnp.bfloat16)
    grad_quarters = lax.psum_scatter(terms, "dx", scatter_dimension=1, tiled=True)
    grad_quarter_in = grad_quarters[0].T
    grad_quarter_out = grad_quarters[1]

    returned = lax.all_to_all(
        expert_out.reshape(expert_count, capacity, width), "expert",
        split_axis=0, concat_axis=0, tiled=True,
    ).reshape(slots, width)
    route_out = lax.dot_general(
        select, returned, contract_first, preferred_element_type=jnp.float32
    )
    weighted = gates.reshape(local_tokens, top_count, 1) * route_out.astype(
        jnp.bfloat16
    ).astype(jnp.float32).reshape(local_tokens, top_count, width)
    mixed = jnp.sum(weighted, axis=1).astype(jnp.bfloat16)
    return (mixed, grad_quarter_in[None], grad_quarter_out[None])


def solution(mesh):
    devices = mesh.devices
    dp_count = devices.shape[0]
    split = Mesh(
        devices.reshape(dp_count // 2, 2, devices.shape[1]), ("dx", "dc", "expert")
    )
    rows = P(("dx", "dc", "expert"), None)
    placed = (
        rows,
        rows,
        rows,
        rows,
        P(),
        P("expert", None, ("dx", "dc")),
        P("expert", ("dx", "dc"), None),
    )
    return jax.shard_map(
        body,
        mesh=split,
        in_specs=placed,
        out_specs=(rows, P("expert", None, ("dx", "dc")), P("expert", ("dx", "dc"), None)),
        check_vma=False,
    )
```

```python
import jax
import jax.numpy as jnp
from jax import lax
from jax.sharding import Mesh, PartitionSpec as P


def partner_2(block, axis, distance):
    count = lax.axis_size(axis)
    route = []
    for low in range(count):
        high = low | 1 << distance
        if high != low and high < count:
            route += [(low, high), (high, low)]
    return lax.ppermute(block, axis, route)


def swap_core(block):
    return lax.ppermute(block, "dc", [(0, 1), (1, 0)])


def body(tokens, cotangent, expert_ids, gates, pair_flags, w_in, w_out):
    expert_count = lax.axis_size("expert")
    own_index = lax.axis_index("expert")
    half_axis = expert_count // 2
    pair_bit = half_axis.bit_length() - 1
    local_tokens, top_count = expert_ids.shape
    width = tokens.shape[1]
    capacity = max(2, 3 * local_tokens * top_count // (2 * expert_count))
    route_count = local_tokens * top_count
    slots = expert_count * capacity
    lanes = jnp.arange(expert_count, dtype=jnp.int32)
    partner = jnp.bitwise_xor(lanes, half_axis * pair_flags)
    flagged = pair_flags[own_index] == 1

    quarter_in = w_in[0].T
    quarter_out = w_out[0]
    their_in, their_out = partner_2((quarter_in, quarter_out), "expert", pair_bit)
    quarter_in = jnp.where(flagged, their_in, quarter_in)
    quarter_out = jnp.where(flagged, their_out, quarter_out)

    flat_ids = expert_ids.reshape(-1)
    target_of = partner[flat_ids]
    onehot = (target_of[:, None] == lanes[None, :]).astype(jnp.int32)
    position = jnp.sum(jnp.cumsum(onehot, axis=0) * onehot, axis=1) - 1
    slot_of = target_of * capacity + position
    select = (slot_of[None, :] == jnp.arange(slots, dtype=jnp.int32)[:, None]).astype(
        jnp.bfloat16
    )
    token_of = jnp.arange(route_count, dtype=jnp.int32) // top_count
    route_rows = tokens[token_of] if top_count > 1 else tokens
    route_cot = cotangent[token_of] if top_count > 1 else cotangent
    scaled = (gates.reshape(-1)[:, None] * route_cot.astype(jnp.float32)).astype(jnp.bfloat16)
    payload = jnp.concatenate([route_rows, scaled], axis=1)
    send = jnp.dot(select, payload, preferred_element_type=jnp.float32).astype(jnp.bfloat16)
    send, quarters = lax.optimization_barrier((send, jnp.stack([quarter_in, quarter_out])))
    halves = lax.all_gather(quarters, "dx", axis=1, tiled=True)
    half_in = halves[0]
    half_out = halves[1]
    recv = lax.all_to_all(
        send.reshape(expert_count, capacity, 2 * width), "expert",
        split_axis=0, concat_axis=0, tiled=True,
    ).reshape(slots, 2 * width)
    other = swap_core(recv)

    contract_last = (((1,), (1,)), ((), ()))
    contract_first = (((0,), (0,)), ((), ()))

    def expert_pass(block):
        rows = block[:, :width]
        grads = block[:, width:]
        pre = lax.dot_general(rows, half_in, contract_last, preferred_element_type=jnp.float32)
        sig = jax.nn.sigmoid(pre)
        hidden = (pre * sig).astype(jnp.bfloat16)
        out = jnp.dot(hidden, half_out, preferred_element_type=jnp.float32)
        dhid = lax.dot_general(grads, half_out, contract_last, preferred_element_type=jnp.float32)
        dpre = (dhid * sig * (1.0 + pre * (1.0 - sig))).astype(jnp.bfloat16)
        term_in = lax.dot_general(dpre, rows, contract_first, preferred_element_type=jnp.float32)
        term_out = lax.dot_general(hidden, grads, contract_first, preferred_element_type=jnp.float32)
        return out, term_in, term_out

    out_other, in_other, outg_other = expert_pass(other)
    back = swap_core(out_other.astype(jnp.bfloat16))
    out_own, in_own, outg_own = expert_pass(recv)
    expert_out = (out_own + back.astype(jnp.float32)).astype(jnp.bfloat16)

    term_out = (outg_own + outg_other).astype(jnp.bfloat16)
    grad_quarter_out = lax.psum_scatter(term_out, "dx", scatter_dimension=0, tiled=True)
    term_in = (in_own + in_other).astype(jnp.bfloat16)
    grad_quarter_in = lax.psum_scatter(term_in, "dx", scatter_dimension=0, tiled=True).T

    returned = lax.all_to_all(
        expert_out.reshape(expert_count, capacity, width), "expert",
        split_axis=0, concat_axis=0, tiled=True,
    ).reshape(slots, width)
    route_out = lax.dot_general(
        select, returned, contract_first, preferred_element_type=jnp.float32
    )
    weighted = gates.reshape(local_tokens, top_count, 1) * route_out.astype(
        jnp.bfloat16
    ).astype(jnp.float32).reshape(local_tokens, top_count, width)
    mixed = jnp.sum(weighted, axis=1).astype(jnp.bfloat16)
    return (mixed, grad_quarter_in[None], grad_quarter_out[None])


def solution(mesh):
    devices = mesh.devices
    dp_count = devices.shape[0]
    split = Mesh(
        devices.reshape(dp_count // 2, 2, devices.shape[1]), ("dx", "dc", "expert")
    )
    rows = P(("dx", "dc", "expert"), None)
    placed = (
        rows,
        rows,
        rows,
        rows,
        P(),
        P("expert", None, ("dx", "dc")),
        P("expert", ("dx", "dc"), None),
    )
    return jax.shard_map(
        body,
        mesh=split,
        in_specs=placed,
        out_specs=(rows, P("expert", None, ("dx", "dc")), P("expert", ("dx", "dc"), None)),
        check_vma=False,
    )
```

```python
import jax
import jax.numpy as jnp
from jax import lax
from jax.sharding import Mesh, PartitionSpec as P


def partner_2(block, axis, distance):
    count = lax.axis_size(axis)
    route = []
    for low in range(count):
        high = low | 1 << distance
        if high != low and high < count:
            route += [(low, high), (high, low)]
    return lax.ppermute(block, axis, route)


def swap_core(block):
    return lax.ppermute(block, "dc", [(0, 1), (1, 0)])


def body(tokens, cotangent, expert_ids, gates, pair_flags, w_in, w_out):
    expert_count = lax.axis_size("expert")
    own_index = lax.axis_index("expert")
    half_axis = expert_count // 2
    pair_bit = half_axis.bit_length() - 1
    local_tokens, top_count = expert_ids.shape
    width = tokens.shape[1]
    capacity = max(2, 3 * local_tokens * top_count // (2 * expert_count))
    route_count = local_tokens * top_count
    slots = expert_count * capacity
    lanes = jnp.arange(expert_count, dtype=jnp.int32)
    partner = jnp.bitwise_xor(lanes, half_axis * pair_flags)
    flagged = pair_flags[own_index] == 1

    quarter_in = w_in[0].T
    quarter_out = w_out[0]
    their_in, their_out = partner_2((quarter_in, quarter_out), "expert", pair_bit)
    quarter_in = jnp.where(flagged, their_in, quarter_in)
    quarter_out = jnp.where(flagged, their_out, quarter_out)

    flat_ids = expert_ids.reshape(-1)
    target_of = partner[flat_ids]
    onehot = (target_of[:, None] == lanes[None, :]).astype(jnp.int32)
    position = jnp.sum(jnp.cumsum(onehot, axis=0) * onehot, axis=1) - 1
    slot_of = target_of * capacity + position
    select = (slot_of[None, :] == jnp.arange(slots, dtype=jnp.int32)[:, None]).astype(
        jnp.bfloat16
    )
    token_of = jnp.arange(route_count, dtype=jnp.int32) // top_count
    route_rows = tokens[token_of] if top_count > 1 else tokens
    route_cot = cotangent[token_of] if top_count > 1 else cotangent
    scaled = (gates.reshape(-1)[:, None] * route_cot.astype(jnp.float32)).astype(jnp.bfloat16)
    payload = jnp.concatenate([route_rows, scaled], axis=1)
    send = jnp.dot(select, payload, preferred_element_type=jnp.float32).astype(jnp.bfloat16)
    send, quarters = lax.optimization_barrier((send, jnp.stack([quarter_in, quarter_out])))
    halves = lax.all_gather(quarters, "dx", axis=1, tiled=True)
    half_in = halves[0]
    half_out = halves[1]
    recv = lax.all_to_all(
        send.reshape(expert_count, capacity, 2 * width), "expert",
        split_axis=0, concat_axis=0, tiled=True,
    ).reshape(slots, 2 * width)
    other = swap_core(recv)

    contract_last = (((1,), (1,)), ((), ()))
    contract_first = (((0,), (0,)), ((), ()))

    def expert_pass(block):
        rows = block[:, :width]
        grads = block[:, width:]
        pre = lax.dot_general(rows, half_in, contract_last, preferred_element_type=jnp.float32)
        sig = jax.nn.sigmoid(pre)
        hidden = (pre * sig).astype(jnp.bfloat16)
        out = jnp.dot(hidden, half_out, preferred_element_type=jnp.float32)
        dhid = lax.dot_general(grads, half_out, contract_last, preferred_element_type=jnp.float32)
        dpre = (dhid * sig * (1.0 + pre * (1.0 - sig))).astype(jnp.bfloat16)
        term_in = lax.dot_general(dpre, rows, contract_first, preferred_element_type=jnp.float32)
        term_out = lax.dot_general(hidden, grads, contract_first, preferred_element_type=jnp.float32)
        return out, term_in, term_out

    out_other, in_other, outg_other = expert_pass(other)
    back = swap_core(out_other.astype(jnp.bfloat16))
    out_own, in_own, outg_own = expert_pass(recv)
    expert_out = (out_own + back.astype(jnp.float32)).astype(jnp.bfloat16)

    term_out = (outg_own + outg_other).astype(jnp.bfloat16)
    grad_quarter_out = lax.psum_scatter(term_out, "dx", scatter_dimension=0, tiled=True)
    term_in = in_own + in_other
    quarter = term_in.shape[0] // 2
    first = lax.axis_index("dx") == 0
    kept = jnp.where(first, term_in[:quarter], term_in[quarter:])
    sent = jnp.where(first, term_in[quarter:], term_in[:quarter]).astype(jnp.bfloat16)
    got = lax.ppermute(sent, "dx", [(0, 1), (1, 0)])
    grad_quarter_in = (kept + got.astype(jnp.float32)).astype(jnp.bfloat16).T

    returned = lax.all_to_all(
        expert_out.reshape(expert_count, capacity, width), "expert",
        split_axis=0, concat_axis=0, tiled=True,
    ).reshape(slots, width)
    route_out = lax.dot_general(
        select, returned, contract_first, preferred_element_type=jnp.float32
    )
    weighted = gates.reshape(local_tokens, top_count, 1) * route_out.astype(
        jnp.bfloat16
    ).astype(jnp.float32).reshape(local_tokens, top_count, width)
    mixed = jnp.sum(weighted, axis=1).astype(jnp.bfloat16)
    return (mixed, grad_quarter_in[None], grad_quarter_out[None])


def solution(mesh):
    devices = mesh.devices
    dp_count = devices.shape[0]
    split = Mesh(
        devices.reshape(dp_count // 2, 2, devices.shape[1]), ("dx", "dc", "expert")
    )
    rows = P(("dx", "dc", "expert"), None)
    placed = (
        rows,
        rows,
        rows,
        rows,
        P(),
        P("expert", None, ("dx", "dc")),
        P("expert", ("dx", "dc"), None),
    )
    return jax.shard_map(
        body,
        mesh=split,
        in_specs=placed,
        out_specs=(rows, P("expert", None, ("dx", "dc")), P("expert", ("dx", "dc"), None)),
        check_vma=False,
    )
```

```python
import jax
import jax.numpy as jnp
from jax import lax
from jax.sharding import Mesh, PartitionSpec as P


def partner_2(block, axis, distance):
    count = lax.axis_size(axis)
    route = []
    for low in range(count):
        high = low | 1 << distance
        if high != low and high < count:
            route += [(low, high), (high, low)]
    return lax.ppermute(block, axis, route)


def swap_core(block):
    return lax.ppermute(block, "dc", [(0, 1), (1, 0)])


def body(tokens, cotangent, expert_ids, gates, pair_flags, w_in, w_out):
    expert_count = lax.axis_size("expert")
    own_index = lax.axis_index("expert")
    half_axis = expert_count // 2
    pair_bit = half_axis.bit_length() - 1
    local_tokens, top_count = expert_ids.shape
    width = tokens.shape[1]
    capacity = max(2, 3 * local_tokens * top_count // (2 * expert_count))
    route_count = local_tokens * top_count
    slots = expert_count * capacity
    lanes = jnp.arange(expert_count, dtype=jnp.int32)
    partner = jnp.bitwise_xor(lanes, half_axis * pair_flags)
    flagged = pair_flags[own_index] == 1

    quarter_in = w_in[0].T
    quarter_out = w_out[0]
    their_in, their_out = partner_2((quarter_in, quarter_out), "expert", pair_bit)
    quarter_in = jnp.where(flagged, their_in, quarter_in)
    quarter_out = jnp.where(flagged, their_out, quarter_out)

    flat_ids = expert_ids.reshape(-1)
    target_of = partner[flat_ids]
    onehot = (target_of[:, None] == lanes[None, :]).astype(jnp.int32)
    position = jnp.sum(jnp.cumsum(onehot, axis=0) * onehot, axis=1) - 1
    slot_of = target_of * capacity + position
    select = (slot_of[None, :] == jnp.arange(slots, dtype=jnp.int32)[:, None]).astype(
        jnp.bfloat16
    )
    token_of = jnp.arange(route_count, dtype=jnp.int32) // top_count
    route_rows = tokens[token_of] if top_count > 1 else tokens
    route_cot = cotangent[token_of] if top_count > 1 else cotangent
    scaled = (gates.reshape(-1)[:, None] * route_cot.astype(jnp.float32)).astype(jnp.bfloat16)
    payload = jnp.concatenate([route_rows, scaled], axis=1)
    send = jnp.dot(select, payload, preferred_element_type=jnp.float32).astype(jnp.bfloat16)
    send, quarters = lax.optimization_barrier((send, jnp.stack([quarter_in, quarter_out])))
    halves = lax.all_gather(quarters, "dx", axis=1, tiled=True)
    half_in = halves[0]
    half_out = halves[1]
    recv = lax.all_to_all(
        send.reshape(expert_count, capacity, 2 * width), "expert",
        split_axis=0, concat_axis=0, tiled=True,
    ).reshape(slots, 2 * width)
    other = swap_core(recv)

    contract_last = (((1,), (1,)), ((), ()))
    contract_first = (((0,), (0,)), ((), ()))

    def expert_pass(block):
        rows = block[:, :width]
        grads = block[:, width:]
        pre = lax.dot_general(rows, half_in, contract_last, preferred_element_type=jnp.float32)
        sig = jax.nn.sigmoid(pre)
        hidden = (pre * sig).astype(jnp.bfloat16)
        out = jnp.dot(hidden, half_out, preferred_element_type=jnp.float32)
        dhid = lax.dot_general(grads, half_out, contract_last, preferred_element_type=jnp.float32)
        dpre = (dhid * sig * (1.0 + pre * (1.0 - sig))).astype(jnp.bfloat16)
        term_in = lax.dot_general(dpre, rows, contract_first, preferred_element_type=jnp.float32)
        term_out = lax.dot_general(hidden, grads, contract_first, preferred_element_type=jnp.float32)
        return out, term_in, term_out

    out_own, in_own, outg_own = expert_pass(recv)
    other, out_own = lax.optimization_barrier((other, out_own))
    out_other, in_other, outg_other = expert_pass(other)
    back = swap_core(out_other.astype(jnp.bfloat16))
    expert_out = (out_own + back.astype(jnp.float32)).astype(jnp.bfloat16)

    term_out = (outg_own + outg_other).astype(jnp.bfloat16)
    grad_quarter_out = lax.psum_scatter(term_out, "dx", scatter_dimension=0, tiled=True)
    term_in = in_own + in_other
    quarter = term_in.shape[0] // 2
    first = lax.axis_index("dx") == 0
    kept = jnp.where(first, term_in[:quarter], term_in[quarter:])
    sent = jnp.where(first, term_in[quarter:], term_in[:quarter]).astype(jnp.bfloat16)
    got = lax.ppermute(sent, "dx", [(0, 1), (1, 0)])
    grad_quarter_in = (kept + got.astype(jnp.float32)).astype(jnp.bfloat16).T

    returned = lax.all_to_all(
        expert_out.reshape(expert_count, capacity, width), "expert",
        split_axis=0, concat_axis=0, tiled=True,
    ).reshape(slots, width)
    route_out = lax.dot_general(
        select, returned, contract_first, preferred_element_type=jnp.float32
    )
    weighted = gates.reshape(local_tokens, top_count, 1) * route_out.astype(
        jnp.bfloat16
    ).astype(jnp.float32).reshape(local_tokens, top_count, width)
    mixed = jnp.sum(weighted, axis=1).astype(jnp.bfloat16)
    return (mixed, grad_quarter_in[None], grad_quarter_out[None])


def solution(mesh):
    devices = mesh.devices
    dp_count = devices.shape[0]
    split = Mesh(
        devices.reshape(dp_count // 2, 2, devices.shape[1]), ("dx", "dc", "expert")
    )
    rows = P(("dx", "dc", "expert"), None)
    placed = (
        rows,
        rows,
        rows,
        rows,
        P(),
        P("expert", None, ("dx", "dc")),
        P("expert", ("dx", "dc"), None),
    )
    return jax.shard_map(
        body,
        mesh=split,
        in_specs=placed,
        out_specs=(rows, P("expert", None, ("dx", "dc")), P("expert", ("dx", "dc"), None)),
        check_vma=False,
    )
```

```python
import jax
import jax.numpy as jnp
from jax import lax
from jax.sharding import Mesh, PartitionSpec as P


def partner_2(block, axis, distance):
    count = lax.axis_size(axis)
    route = []
    for low in range(count):
        high = low | 1 << distance
        if high != low and high < count:
            route += [(low, high), (high, low)]
    return lax.ppermute(block, axis, route)


def swap_core(block):
    return lax.ppermute(block, "dc", [(0, 1), (1, 0)])


def body(tokens, cotangent, expert_ids, gates, pair_flags, w_in, w_out):
    expert_count = lax.axis_size("expert")
    own_index = lax.axis_index("expert")
    half_axis = expert_count // 2
    pair_bit = half_axis.bit_length() - 1
    local_tokens, top_count = expert_ids.shape
    width = tokens.shape[1]
    capacity = max(2, 3 * local_tokens * top_count // (2 * expert_count))
    route_count = local_tokens * top_count
    slots = expert_count * capacity
    lanes = jnp.arange(expert_count, dtype=jnp.int32)
    partner = jnp.bitwise_xor(lanes, half_axis * pair_flags)
    flagged = pair_flags[own_index] == 1

    quarter_in = w_in[0].T
    quarter_out = w_out[0]
    their_in, their_out = partner_2((quarter_in, quarter_out), "expert", pair_bit)
    quarter_in = jnp.where(flagged, their_in, quarter_in)
    quarter_out = jnp.where(flagged, their_out, quarter_out)

    flat_ids = expert_ids.reshape(-1)
    target_of = partner[flat_ids]
    onehot = (target_of[:, None] == lanes[None, :]).astype(jnp.int32)
    position = jnp.sum(jnp.cumsum(onehot, axis=0) * onehot, axis=1) - 1
    slot_of = target_of * capacity + position
    select = (slot_of[None, :] == jnp.arange(slots, dtype=jnp.int32)[:, None]).astype(
        jnp.bfloat16
    )
    token_of = jnp.arange(route_count, dtype=jnp.int32) // top_count
    route_rows = tokens[token_of] if top_count > 1 else tokens
    route_cot = cotangent[token_of] if top_count > 1 else cotangent
    scaled = (gates.reshape(-1)[:, None] * route_cot.astype(jnp.float32)).astype(jnp.bfloat16)
    payload = jnp.concatenate([route_rows, scaled], axis=1)
    send = jnp.dot(select, payload, preferred_element_type=jnp.float32).astype(jnp.bfloat16)
    send, quarters = lax.optimization_barrier((send, jnp.stack([quarter_in, quarter_out])))
    halves = lax.all_gather(quarters, "dx", axis=1, tiled=True)
    half_in = halves[0]
    half_out = halves[1]
    recv = lax.all_to_all(
        send.reshape(expert_count, capacity, 2 * width), "expert",
        split_axis=0, concat_axis=0, tiled=True,
    ).reshape(slots, 2 * width)
    other = swap_core(recv)

    contract_last = (((1,), (1,)), ((), ()))
    contract_first = (((0,), (0,)), ((), ()))

    def expert_pass(block):
        rows = block[:, :width]
        grads = block[:, width:]
        pre = lax.dot_general(rows, half_in, contract_last, preferred_element_type=jnp.float32)
        sig = jax.nn.sigmoid(pre)
        hidden = (pre * sig).astype(jnp.bfloat16)
        out = jnp.dot(hidden, half_out, preferred_element_type=jnp.float32)
        dhid = lax.dot_general(grads, half_out, contract_last, preferred_element_type=jnp.float32)
        dpre = (dhid * sig * (1.0 + pre * (1.0 - sig))).astype(jnp.bfloat16)
        term_in = lax.dot_general(dpre, rows, contract_first, preferred_element_type=jnp.float32)
        term_out = lax.dot_general(hidden, grads, contract_first, preferred_element_type=jnp.float32)
        return out, term_in, term_out

    out_own, in_own, outg_own = expert_pass(recv)
    other, out_own = lax.optimization_barrier((other, out_own))
    out_other, in_other, outg_other = expert_pass(other)
    back = swap_core(out_other.astype(jnp.bfloat16))
    expert_out = (out_own + back.astype(jnp.float32)).astype(jnp.bfloat16)

    term_out = (outg_own + outg_other).astype(jnp.bfloat16)
    grad_quarter_out = lax.psum_scatter(term_out, "dx", scatter_dimension=0, tiled=True)
    term_in = in_own + in_other
    quarter = term_in.shape[0] // 2
    first = lax.axis_index("dx") == 0
    kept = jnp.where(first, term_in[:quarter], term_in[quarter:])
    sent = jnp.where(first, term_in[quarter:], term_in[:quarter]).astype(jnp.bfloat16)
    got = lax.ppermute(sent, "dx", [(0, 1), (1, 0)])
    grad_quarter_in = (kept + got.astype(jnp.float32)).astype(jnp.bfloat16).T

    returned = lax.all_to_all(
        expert_out.reshape(expert_count, capacity, width), "expert",
        split_axis=0, concat_axis=0, tiled=True,
    )
    route_out = lax.dot_general(
        select.reshape(expert_count, capacity, route_count), returned,
        (((0, 1), (0, 1)), ((), ())), preferred_element_type=jnp.float32,
    )
    weighted = gates.reshape(local_tokens, top_count, 1) * route_out.astype(
        jnp.bfloat16
    ).astype(jnp.float32).reshape(local_tokens, top_count, width)
    mixed = jnp.sum(weighted, axis=1).astype(jnp.bfloat16)
    return (mixed, grad_quarter_in[None], grad_quarter_out[None])


def solution(mesh):
    devices = mesh.devices
    dp_count = devices.shape[0]
    split = Mesh(
        devices.reshape(dp_count // 2, 2, devices.shape[1]), ("dx", "dc", "expert")
    )
    rows = P(("dx", "dc", "expert"), None)
    placed = (
        rows,
        rows,
        rows,
        rows,
        P(),
        P("expert", None, ("dx", "dc")),
        P("expert", ("dx", "dc"), None),
    )
    return jax.shard_map(
        body,
        mesh=split,
        in_specs=placed,
        out_specs=(rows, P("expert", None, ("dx", "dc")), P("expert", ("dx", "dc"), None)),
        check_vma=False,
    )
```
